256 devices in a mesh: dp: 16 (over z, core), tensor: 16 (over y, x).
Axes of the slice: x: 4, y: 4, z: 8, core: 2. Of those that a mesh axis runs over, the one named last changes fastest.
Arguments:
- hidden_rows: bfloat16 [16384, 3584], P(('dp', 'tensor')), parts along dimension 0, may hold values from -48 to 48
- norm_gain: float32 [3584], replicated, may hold values from 0.5 to 2
- gate_weight: bfloat16 [9216, 3584], P('tensor'), may hold values from -0.09375 to 0.09375
- up_weight: bfloat16 [9216, 3584], P('tensor'), may hold values from -0.09375 to 0.09375
- down_weight: bfloat16 [9216, 3584], P('tensor'), may hold values from -0.0625 to 0.0625
- span_lengths: int32 [256], P('dp'), parts along dimension 0, may hold values from 1 to 64, 512 in all
Outputs:
- ffn_out: bfloat16 [16384, 3584], P(('dp', 'tensor')), parts along dimension 0
The draws below stay inside these ranges and needn't reach their ends.
There are 16 independent parts, one for each index of `dp`. The reference program is written for one: setup_inputs(seed, part) draws one part's arguments, and reference() takes and returns one part's arrays. A program takes and returns all parts, laid end to end along the dimension named above; an argument that names none is the same for every part. Nothing has to cross between parts.
Inputs may be any that keep to these rules, and one draw needn't show every extreme that they name: `span_lengths`: the lengths of one part sum to exactly 512, and the largest is exactly 64.
All inputs are finite; a program needn't handle non-finite values.
Results may differ from the reference program's by a relative error of at most 0.0065.
Values may be sent and summed in bfloat16 or wider, within the bound.
No kernel may reach another device: no remote copies, remote signals or barrier semaphores. Data moves between devices by JAX's collectives and lax.ppermute only.
A program may use at most 128 MiB of HBM per device.

```python
import math
import jax
import jax.numpy as jnp
import numpy as np
from jax import lax

D = 3584
FF = 9216
SPAN_CAP = 64
TOKENS = 1024
TOTAL = 512
N_TENSOR = 16


def draw_hidden_rows(key, part):
    first, second, third = jax.random.split(key, 3)
    base = jnp.clip(jax.random.normal(first, (TOKENS, D), jnp.float32), -4.0, 4.0)
    row_scale = jnp.exp(jax.random.uniform(second, (TOKENS, 1), jnp.float32, math.log(0.3), math.log(3.0)))
    column_scale = jnp.exp(jax.random.uniform(third, (1, D), jnp.float32, math.log(0.3), math.log(3.0)))
    return (base * row_scale * column_scale).astype(jnp.bfloat16)


def shard_levels(rng, shape, cuts, low, largest):
    def one(dim, parts):
        steps = jax.random.uniform(jax.random.fold_in(jax.random.fold_in(rng, 6), dim), (parts,), jnp.float32, low / len(cuts), largest / len(cuts))
        return jnp.repeat(jnp.exp(steps), shape[dim] // parts).reshape((-1,) + (1,) * (len(shape) - dim - 1))

    loudness = one(*cuts[0])
    for cut in cuts[1:]:
        loudness = loudness * one(*cut)
    return loudness


def length_profile(count, total, reach, slope):
    loads = [(1 << 20) // math.isqrt(standing ** slope) + 1 for standing in range(2, count + 1)]
    rest, holding = total - reach - (count - 1), [1] * (count - 1)
    while rest > 0:
        movable = [i for i in range(count - 1) if holding[i] < reach]
        pool, remaining = sum([loads[i] for i in movable]), rest
        for i in movable:
            addition = min(reach - holding[i], max(1, remaining * loads[i] // pool), rest)
            holding[i] = holding[i] + addition
            rest = rest - addition
    return np.array([reach] + holding)


def uneven_parts(own_key, number_of, total, bound, lean):
    if number_of == 2:
        one = jax.random.randint(own_key, (), max(1, total - bound), min(bound, total - 1) + 1)
        return jnp.stack([one, total - one])
    lengths = jnp.asarray(length_profile(number_of, total, bound, lean), jnp.int32)
    twos = (number_of - 1) // 2
    giver, receiver = lengths[1:1 + 2 * twos:2], lengths[2:2 + 2 * twos:2]
    room = jnp.minimum(giver - 1, bound - receiver)
    moved = jax.random.randint(jax.random.fold_in(own_key, 1), (twos,), 0, 1 << 20) % (room + 1)
    lengths = lengths.at[1:1 + 2 * twos:2].set(giver - moved).at[2:2 + 2 * twos:2].set(receiver + moved)
    return lengths[jax.random.permutation(jax.random.fold_in(own_key, 2), number_of)]


def gaussian(own_key, extent, width, limit, cuts=(), held_as=jnp.bfloat16):
    factor_of = shard_levels(own_key, extent, cuts, -0.22, 0.18) if cuts else 1.0
    result = jax.random.normal(own_key, extent, jnp.float32) * width * factor_of
    return jnp.minimum(jnp.maximum(result, -limit), limit).astype(held_as)


def setup_inputs(seed: int = 0, part: int = 0) -> dict:
    seeds = jax.random.split(jax.random.key(seed), 7)
    own_keys = jax.random.split(jax.random.fold_in(seeds[6], part), 7)
    return {
        "hidden_rows": draw_hidden_rows(jax.random.fold_in(jax.random.fold_in(seeds[6], part), 71), part),
        "norm_gain": jnp.clip(jnp.exp(jax.random.uniform(seeds[1], (D,), jnp.float32, math.log(0.5), math.log(2.0))), 0.5, 2.0),
        "gate_weight": gaussian(seeds[2], (FF, D), D ** -0.5, 0.09375, ((0, 16),)),
        "up_weight": gaussian(seeds[3], (FF, D), D ** -0.5, 0.09375, ((0, 16),)),
        "down_weight": gaussian(seeds[4], (FF, D), FF ** -0.5, 0.0625, ((0, 16),)),
        "span_lengths": uneven_parts(own_keys[5], N_TENSOR, TOTAL, SPAN_CAP, 2).astype(jnp.int32),
    }


def reference(hidden_rows, norm_gain, gate_weight, up_weight, down_weight, span_lengths):
    widened = hidden_rows.astype(jnp.float32)
    scale = lax.rsqrt(lax.optimization_barrier(jnp.mean(widened * widened, axis=-1, keepdims=True)) + 1e-06)
    normed = (widened * scale * norm_gain).astype(jnp.bfloat16)
    dims = (((1,), (1,)), ((), ()))
    gate_part = lax.dot_general(normed, gate_weight, dims, preferred_element_type=jnp.float32)
    up_part = lax.dot_general(normed, up_weight, dims, preferred_element_type=jnp.float32)
    hidden = (jax.nn.silu(gate_part) * up_part).astype(jnp.bfloat16)
    summed = jnp.dot(hidden, down_weight, preferred_element_type=jnp.float32).astype(jnp.bfloat16)
    row_ids = jnp.arange(hidden_rows.shape[0], dtype=jnp.int32)
    owner_rank = row_ids // SPAN_CAP
    limits = jnp.take(span_lengths, owner_rank)
    live_mask = row_ids % SPAN_CAP < limits
    return jnp.where(live_mask[:, None], summed, jnp.zeros_like(summed))
```

```python
import jax
import jax.numpy as jnp
from jax import lax
from jax.sharding import PartitionSpec as P

NX = 4


def _shift(n, axis, step):
    ny = n // NX
    pairs = []
    for t in range(n):
        y, x = divmod(t, NX)
        if axis == "x":
            d = y * NX + (x + step) % NX
        else:
            d = ((y + step) % ny) * NX + x
        pairs.append((t, d))
    return pairs


def _gather_ring(s, n, axis):
    ahead = lax.ppermute(s, "tensor", _shift(n, axis, -1))
    behind = lax.ppermute(s, "tensor", _shift(n, axis, +1))
    h = s.shape[-2] // 2
    far_lo = lax.ppermute(behind[..., :h, :], "tensor", _shift(n, axis, +1))
    far_hi = lax.ppermute(ahead[..., h:, :], "tensor", _shift(n, axis, -1))
    far = jnp.concatenate([far_lo, far_hi], axis=-2)
    return jnp.stack([s, ahead, far, behind])


def _reduce_ring(c, n, axis):
    h = c.shape[-2] // 2

    def ring(part, step, order):
        perm = _shift(n, axis, step)
        r = lax.ppermute(part[order[0]].astype(jnp.bfloat16), "tensor", perm)
        r = lax.ppermute((r.astype(jnp.float32) + part[order[1]]).astype(jnp.bfloat16), "tensor", perm)
        r = lax.ppermute((r.astype(jnp.float32) + part[order[2]]).astype(jnp.bfloat16), "tensor", perm)
        return r.astype(jnp.float32) + part[0]

    lo = ring(c[..., :h, :], +1, (3, 2, 1))
    hi = ring(c[..., h:, :], -1, (1, 2, 3))
    return jnp.concatenate([lo, hi], axis=-2)


def _ffn(rows, gate_weight, up_weight, down_weight):
    dims = (((1,), (1,)), ((), ()))
    gate = lax.dot_general(rows, gate_weight, dims, preferred_element_type=jnp.float32)
    up = lax.dot_general(rows, up_weight, dims, preferred_element_type=jnp.float32)
    act = (jax.nn.silu(gate) * up).astype(jnp.bfloat16)
    return jnp.dot(act, down_weight, preferred_element_type=jnp.float32)


def shards(hidden_rows, norm_gain, gate_weight, up_weight, down_weight, span_lengths):
    capacity, width = hidden_rows.shape
    n = span_lengths.shape[0]
    ny = n // NX
    own_rank = lax.axis_index("tensor")
    widened = hidden_rows.astype(jnp.float32)
    scale = lax.rsqrt(jnp.mean(widened * widened, axis=-1, keepdims=True) + 1e-06)
    normed = (widened * scale * norm_gain).astype(jnp.bfloat16)

    half = capacity // 2
    a_x = _gather_ring(normed[:half], n, "x")
    b_y = _gather_ring(normed[half:], n, "y")
    a_yx = _gather_ring(a_x, n, "y")
    b_xy = _gather_ring(b_y, n, "x")

    out_a = _ffn(a_yx.reshape(-1, width), gate_weight, up_weight, down_weight)
    out_b = _ffn(b_xy.reshape(-1, width), gate_weight, up_weight, down_weight)
    out_a = out_a.reshape(ny, NX, half, width)
    out_b = out_b.reshape(NX, ny, half, width)

    sum_a = _reduce_ring(_reduce_ring(out_a, n, "y"), n, "x")
    sum_b = _reduce_ring(_reduce_ring(out_b, n, "x"), n, "y")
    result = jnp.concatenate([sum_a, sum_b], axis=0).astype(jnp.bfloat16)
    live_mask = jnp.arange(capacity, dtype=jnp.int32) < span_lengths[own_rank]
    return jnp.where(live_mask[:, None], result, jnp.zeros_like(result))


def solution(mesh):
    return jax.shard_map(
        shards,
        mesh=mesh,
        in_specs=(
            P(("dp", "tensor"), None),
            P(),
            P("tensor", None),
            P("tensor", None),
            P("tensor", None),
            P("dp"),
        ),
        out_specs=P(("dp", "tensor"), None),
        check_vma=False,
    )
```

```python
import jax
import jax.numpy as jnp
from jax import lax
from jax.sharding import PartitionSpec as P

NX = 4


def _shift(n, axis, step):
    ny = n // NX
    pairs = []
    for t in range(n):
        y, x = divmod(t, NX)
        if axis == "x":
            d = y * NX + (x + step) % NX
        else:
            d = ((y + step) % ny) * NX + x
        pairs.append((t, d))
    return pairs


def _gather_ring(s, n, axis):
    ahead = lax.ppermute(s, "tensor", _shift(n, axis, -1))
    behind = lax.ppermute(s, "tensor", _shift(n, axis, +1))
    h = s.shape[-2] // 2
    far_lo = lax.ppermute(behind[..., :h, :], "tensor", _shift(n, axis, +1))
    far_hi = lax.ppermute(ahead[..., h:, :], "tensor", _shift(n, axis, -1))
    far = jnp.concatenate([far_lo, far_hi], axis=-2)
    return jnp.stack([s, ahead, far, behind])


def _reduce_relay(c, n, axis):
    h = c.shape[-2] // 2
    lo, hi = (lambda v: v[..., :h, :]), (lambda v: v[..., h:, :])
    bf, f32 = jnp.bfloat16, jnp.float32
    up, down = _shift(n, axis, +1), _shift(n, axis, -1)
    from_behind = lax.ppermute(jnp.concatenate([lo(c[1]), hi(c[2])], axis=-2).astype(bf), "tensor", up)
    from_ahead = lax.ppermute(jnp.concatenate([lo(c[2]), hi(c[3])], axis=-2).astype(bf), "tensor", down)
    relay_up = (hi(c[1]).astype(f32) + hi(from_behind).astype(f32)).astype(bf)
    relay_down = (lo(c[3]).astype(f32) + lo(from_ahead).astype(f32)).astype(bf)
    second_behind = lax.ppermute(relay_up, "tensor", up)
    second_ahead = lax.ppermute(relay_down, "tensor", down)
    own = c[0].astype(f32)
    sum_lo = lo(own) + lo(from_behind).astype(f32) + second_ahead.astype(f32)
    sum_hi = hi(own) + hi(from_ahead).astype(f32) + second_behind.astype(f32)
    return jnp.concatenate([sum_lo, sum_hi], axis=-2)


def _ffn(rows, gate_weight, up_weight, down_weight):
    dims = (((1,), (1,)), ((), ()))
    gate = lax.dot_general(rows, gate_weight, dims, preferred_element_type=jnp.float32)
    up = lax.dot_general(rows, up_weight, dims, preferred_element_type=jnp.float32)
    act = (jax.nn.silu(gate) * up).astype(jnp.bfloat16)
    return jnp.dot(act, down_weight, preferred_element_type=jnp.float32).astype(jnp.bfloat16)


def shards(hidden_rows, norm_gain, gate_weight, up_weight, down_weight, span_lengths):
    capacity, width = hidden_rows.shape
    n = span_lengths.shape[0]
    ny = n // NX
    own_rank = lax.axis_index("tensor")
    widened = hidden_rows.astype(jnp.float32)
    scale = lax.rsqrt(jnp.mean(widened * widened, axis=-1, keepdims=True) + 1e-06)
    normed = (widened * scale * norm_gain).astype(jnp.bfloat16)

    half = capacity // 2
    a_x = _gather_ring(normed[:half], n, "x")
    b_y = _gather_ring(normed[half:], n, "y")
    a_yx = _gather_ring(a_x, n, "y")
    b_xy = _gather_ring(b_y, n, "x")

    out_a = _ffn(a_yx.reshape(-1, width), gate_weight, up_weight, down_weight)
    out_b = _ffn(b_xy.reshape(-1, width), gate_weight, up_weight, down_weight)
    out_a = out_a.reshape(ny, NX, half, width)
    out_b = out_b.reshape(NX, ny, half, width)

    sum_a = _reduce_relay(_reduce_relay(out_a, n, "y"), n, "x")
    sum_b = _reduce_relay(_reduce_relay(out_b, n, "x"), n, "y")
    result = jnp.concatenate([sum_a, sum_b], axis=0).astype(jnp.bfloat16)
    live_mask = jnp.arange(capacity, dtype=jnp.int32) < span_lengths[own_rank]
    return jnp.where(live_mask[:, None], result, jnp.zeros_like(result))


def solution(mesh):
    return jax.shard_map(
        shards,
        mesh=mesh,
        in_specs=(
            P(("dp", "tensor"), None),
            P(),
            P("tensor", None),
            P("tensor", None),
            P("tensor", None),
            P("dp"),
        ),
        out_specs=P(("dp", "tensor"), None),
        check_vma=False,
    )
```

```python
import jax
import jax.numpy as jnp
from jax import lax
from jax.sharding import PartitionSpec as P

NX = 4


def _shift(n, axis, step):
    ny = n // NX
    pairs = []
    for t in range(n):
        y, x = divmod(t, NX)
        if axis == "x":
            d = y * NX + (x + step) % NX
        else:
            d = ((y + step) % ny) * NX + x
        pairs.append((t, d))
    return pairs


def _gather_ring(s, n, axis):
    ahead = lax.ppermute(s, "tensor", _shift(n, axis, -1))
    behind = lax.ppermute(s, "tensor", _shift(n, axis, +1))
    h = s.shape[-2] // 2
    far_lo = lax.ppermute(behind[..., :h, :], "tensor", _shift(n, axis, +1))
    far_hi = lax.ppermute(ahead[..., h:, :], "tensor", _shift(n, axis, -1))
    far = jnp.concatenate([far_lo, far_hi], axis=-2)
    return jnp.stack([s, ahead, far, behind])


def _reduce_relay(c, n, axis):
    h = c.shape[-2] // 2
    lo, hi = (lambda v: v[..., :h, :]), (lambda v: v[..., h:, :])
    bf, f32 = jnp.bfloat16, jnp.float32
    up, down = _shift(n, axis, +1), _shift(n, axis, -1)
    from_behind = lax.ppermute(jnp.concatenate([lo(c[1]), hi(c[2])], axis=-2).astype(bf), "tensor", up)
    from_ahead = lax.ppermute(jnp.concatenate([lo(c[2]), hi(c[3])], axis=-2).astype(bf), "tensor", down)
    relay_up = (hi(c[1]).astype(f32) + hi(from_behind).astype(f32)).astype(bf)
    relay_down = (lo(c[3]).astype(f32) + lo(from_ahead).astype(f32)).astype(bf)
    second_behind = lax.ppermute(relay_up, "tensor", up)
    second_ahead = lax.ppermute(relay_down, "tensor", down)
    own = c[0].astype(f32)
    sum_lo = lo(own) + lo(from_behind).astype(f32) + second_ahead.astype(f32)
    sum_hi = hi(own) + hi(from_ahead).astype(f32) + second_behind.astype(f32)
    return jnp.concatenate([sum_lo, sum_hi], axis=-2)


def _ffn(rows, gate_weight, up_weight, down_weight):
    dims = (((1,), (1,)), ((), ()))
    gate = lax.dot_general(rows, gate_weight, dims, preferred_element_type=jnp.float32)
    up = lax.dot_general(rows, up_weight, dims, preferred_element_type=jnp.float32)
    act = (jax.nn.silu(gate) * up).astype(jnp.bfloat16)
    act = lax.optimization_barrier(act)
    return jnp.dot(act, down_weight, preferred_element_type=jnp.float32).astype(jnp.bfloat16)


def shards(hidden_rows, norm_gain, gate_weight, up_weight, down_weight, span_lengths):
    capacity, width = hidden_rows.shape
    n = span_lengths.shape[0]
    ny = n // NX
    own_rank = lax.axis_index("tensor")
    widened = hidden_rows.astype(jnp.float32)
    scale = lax.rsqrt(jnp.mean(widened * widened, axis=-1, keepdims=True) + 1e-06)
    normed = (widened * scale * norm_gain).astype(jnp.bfloat16)

    half = capacity // 2
    a_x = _gather_ring(normed[:half], n, "x")
    b_y = _gather_ring(normed[half:], n, "y")
    a_yx = _gather_ring(a_x, n, "y")
    b_xy = _gather_ring(b_y, n, "x")

    out_a = _ffn(a_yx.reshape(-1, width), gate_weight, up_weight, down_weight)
    out_b = _ffn(b_xy.reshape(-1, width), gate_weight, up_weight, down_weight)
    out_a = out_a.reshape(ny, NX, half, width)
    out_b = out_b.reshape(NX, ny, half, width)

    sum_a = _reduce_relay(_reduce_relay(out_a, n, "y"), n, "x")
    sum_b = _reduce_relay(_reduce_relay(out_b, n, "x"), n, "y")
    result = jnp.concatenate([sum_a, sum_b], axis=0).astype(jnp.bfloat16)
    live_mask = jnp.arange(capacity, dtype=jnp.int32) < span_lengths[own_rank]
    return jnp.where(live_mask[:, None], result, jnp.zeros_like(result))


def solution(mesh):
    return jax.shard_map(
        shards,
        mesh=mesh,
        in_specs=(
            P(("dp", "tensor"), None),
            P(),
            P("tensor", None),
            P("tensor", None),
            P("tensor", None),
            P("dp"),
        ),
        out_specs=P(("dp", "tensor"), None),
        check_vma=False,
    )
```

```python
import jax
import jax.numpy as jnp
from jax import lax
from jax.sharding import PartitionSpec as P

NX = 4


def _shift(n, axis, step):
    ny = n // NX
    pairs = []
    for t in range(n):
        y, x = divmod(t, NX)
        if axis == "x":
            d = y * NX + (x + step) % NX
        else:
            d = ((y + step) % ny) * NX + x
        pairs.append((t, d))
    return pairs


def _gather_ring(s, n, axis):
    ahead = lax.ppermute(s, "tensor", _shift(n, axis, -1))
    behind = lax.ppermute(s, "tensor", _shift(n, axis, +1))
    h = s.shape[-2] // 2
    far_lo = lax.ppermute(behind[..., :h, :], "tensor", _shift(n, axis, +1))
    far_hi = lax.ppermute(ahead[..., h:, :], "tensor", _shift(n, axis, -1))
    far = jnp.concatenate([far_lo, far_hi], axis=-2)
    return [s, ahead, far, behind]


def _reduce_relay(c, n, axis):
    h = c[0].shape[-2] // 2
    lo, hi = (lambda v: v[..., :h, :]), (lambda v: v[..., h:, :])
    bf, f32 = jnp.bfloat16, jnp.float32
    up, down = _shift(n, axis, +1), _shift(n, axis, -1)
    from_behind = lax.ppermute(jnp.concatenate([lo(c[1]), hi(c[2])], axis=-2).astype(bf), "tensor", up)
    from_ahead = lax.ppermute(jnp.concatenate([lo(c[2]), hi(c[3])], axis=-2).astype(bf), "tensor", down)
    relay_up = (hi(c[1]).astype(f32) + hi(from_behind).astype(f32)).astype(bf)
    relay_down = (lo(c[3]).astype(f32) + lo(from_ahead).astype(f32)).astype(bf)
    second_behind = lax.ppermute(relay_up, "tensor", up)
    second_ahead = lax.ppermute(relay_down, "tensor", down)
    own = c[0].astype(f32)
    sum_lo = lo(own) + lo(from_behind).astype(f32) + second_ahead.astype(f32)
    sum_hi = hi(own) + hi(from_ahead).astype(f32) + second_behind.astype(f32)
    return jnp.concatenate([sum_lo, sum_hi], axis=-2)


def _ffn(rows, gate_weight, up_weight, down_weight):
    dims = (((1,), (1,)), ((), ()))
    gate = lax.dot_general(rows, gate_weight, dims, preferred_element_type=jnp.float32)
    up = lax.dot_general(rows, up_weight, dims, preferred_element_type=jnp.float32)
    act = (jax.nn.silu(gate) * up).astype(jnp.bfloat16)
    act = lax.optimization_barrier(act)
    return jnp.dot(act, down_weight, preferred_element_type=jnp.float32).astype(jnp.bfloat16)


def shards(hidden_rows, norm_gain, gate_weight, up_weight, down_weight, span_lengths):
    capacity, width = hidden_rows.shape
    n = span_lengths.shape[0]
    own_rank = lax.axis_index("tensor")
    widened = hidden_rows.astype(jnp.float32)
    scale = lax.rsqrt(jnp.mean(widened * widened, axis=-1, keepdims=True) + 1e-06)
    normed = (widened * scale * norm_gain).astype(jnp.bfloat16)

    half = capacity // 2

    def ffn(part):
        return _ffn(part.reshape(-1, width), gate_weight, up_weight, down_weight).reshape(part.shape)

    a_x = jnp.stack(_gather_ring(normed[:half], n, "x"))
    b_y = jnp.stack(_gather_ring(normed[half:], n, "y"))
    out_a = [ffn(p) for p in _gather_ring(a_x, n, "y")]
    out_b = [ffn(p) for p in _gather_ring(b_y, n, "x")]

    sum_a = _reduce_relay(_reduce_relay(out_a, n, "y"), n, "x")
    sum_b = _reduce_relay(_reduce_relay(out_b, n, "x"), n, "y")
    result = jnp.concatenate([sum_a, sum_b], axis=0).astype(jnp.bfloat16)
    live_mask = jnp.arange(capacity, dtype=jnp.int32) < span_lengths[own_rank]
    return jnp.where(live_mask[:, None], result, jnp.zeros_like(result))


def solution(mesh):
    return jax.shard_map(
        shards,
        mesh=mesh,
        in_specs=(
            P(("dp", "tensor"), None),
            P(),
            P("tensor", None),
            P("tensor", None),
            P("tensor", None),
            P("dp"),
        ),
        out_specs=P(("dp", "tensor"), None),
        check_vma=False,
    )
```

```python
import jax
import jax.numpy as jnp
from jax import lax
from jax.sharding import PartitionSpec as P

NX = 4


def _shift(n, axis, step):
    ny = n // NX
    pairs = []
    for t in range(n):
        y, x = divmod(t, NX)
        if axis == "x":
            d = y * NX + (x + step) % NX
        else:
            d = ((y + step) % ny) * NX + x
        pairs.append((t, d))
    return pairs


def _gather_ring(s, n, axis):
    ahead = lax.ppermute(s, "tensor", _shift(n, axis, -1))
    behind = lax.ppermute(s, "tensor", _shift(n, axis, +1))
    h = s.shape[-2] // 2
    far_lo = lax.ppermute(behind[..., :h, :], "tensor", _shift(n, axis, +1))
    far_hi = lax.ppermute(ahead[..., h:, :], "tensor", _shift(n, axis, -1))
    far = jnp.concatenate([far_lo, far_hi], axis=-2)
    return [s, ahead, far, behind]


def _reduce_relay(c, n, axis):
    h = c[0].shape[-2] // 2
    lo, hi = (lambda v: v[..., :h, :]), (lambda v: v[..., h:, :])
    bf, f32 = jnp.bfloat16, jnp.float32
    up, down = _shift(n, axis, +1), _shift(n, axis, -1)
    from_behind = lax.ppermute(jnp.concatenate([lo(c[1]), hi(c[2])], axis=-2).astype(bf), "tensor", up)
    from_ahead = lax.ppermute(jnp.concatenate([lo(c[2]), hi(c[3])], axis=-2).astype(bf), "tensor", down)
    relay_up = (hi(c[1]).astype(f32) + hi(from_behind).astype(f32)).astype(bf)
    relay_down = (lo(c[3]).astype(f32) + lo(from_ahead).astype(f32)).astype(bf)
    second_behind = lax.ppermute(relay_up, "tensor", up)
    second_ahead = lax.ppermute(relay_down, "tensor", down)
    own = c[0].astype(f32)
    sum_lo = lo(own) + lo(from_behind).astype(f32) + second_ahead.astype(f32)
    sum_hi = hi(own) + hi(from_ahead).astype(f32) + second_behind.astype(f32)
    return jnp.concatenate([sum_lo, sum_hi], axis=-2)


def _ffn(rows, gate_weight, up_weight, down_weight):
    dims = (((1,), (1,)), ((), ()))
    gate = lax.dot_general(rows, gate_weight, dims, preferred_element_type=jnp.float32)
    up = lax.dot_general(rows, up_weight, dims, preferred_element_type=jnp.float32)
    act = (jax.nn.silu(gate) * up).astype(jnp.bfloat16)
    act = lax.optimization_barrier(act)
    return jnp.dot(act, down_weight, preferred_element_type=jnp.float32).astype(jnp.bfloat16)


def shards(hidden_rows, norm_gain, gate_weight, up_weight, down_weight, span_lengths):
    capacity, width = hidden_rows.shape
    n = span_lengths.shape[0]
    own_rank = lax.axis_index("tensor")
    widened = hidden_rows.astype(jnp.float32)
    scale = lax.rsqrt(jnp.mean(widened * widened, axis=-1, keepdims=True) + 1e-06)
    normed = (widened * scale * norm_gain).astype(jnp.bfloat16)

    half = capacity // 2

    def ffn(part):
        return _ffn(part.reshape(-1, width), gate_weight, up_weight, down_weight).reshape(part.shape)

    a_x = jnp.stack(_gather_ring(normed[:half], n, "x"))
    b_y = jnp.stack(_gather_ring(normed[half:], n, "y"))
    out_a = [ffn(p) for p in _gather_ring(a_x, n, "y")]
    b_parts = _gather_ring(b_y, n, "x")
    out_a, b_parts = lax.optimization_barrier((out_a, b_parts))
    out_b = [ffn(p) for p in b_parts]

    sum_a = _reduce_relay(_reduce_relay(out_a, n, "y"), n, "x")
    sum_b = _reduce_relay(_reduce_relay(out_b, n, "x"), n, "y")
    result = jnp.concatenate([sum_a, sum_b], axis=0).astype(jnp.bfloat16)
    live_mask = jnp.arange(capacity, dtype=jnp.int32) < span_lengths[own_rank]
    return jnp.where(live_mask[:, None], result, jnp.zeros_like(result))


def solution(mesh):
    return jax.shard_map(
        shards,
        mesh=mesh,
        in_specs=(
            P(("dp", "tensor"), None),
            P(),
            P("tensor", None),
            P("tensor", None),
            P("tensor", None),
            P("dp"),
        ),
        out_specs=P(("dp", "tensor"), None),
        check_vma=False,
    )
```

```python
import jax
import jax.numpy as jnp
from jax import lax
from jax.sharding import PartitionSpec as P

NX = 4


def _shift(n, axis, step):
    ny = n // NX
    pairs = []
    for t in range(n):
        y, x = divmod(t, NX)
        if axis == "x":
            d = y * NX + (x + step) % NX
        else:
            d = ((y + step) % ny) * NX + x
        pairs.append((t, d))
    return pairs


def _gather_ring(s, n, axis):
    ahead = lax.ppermute(s, "tensor", _shift(n, axis, -1))
    behind = lax.ppermute(s, "tensor", _shift(n, axis, +1))
    h = s.shape[-2] // 2
    far_lo = lax.ppermute(behind[..., :h, :], "tensor", _shift(n, axis, +1))
    far_hi = lax.ppermute(ahead[..., h:, :], "tensor", _shift(n, axis, -1))
    far = jnp.concatenate([far_lo, far_hi], axis=-2)
    return [s, ahead, far, behind]


def _reduce_relay(c, n, axis):
    h = c[0].shape[-2] // 2
    lo, hi = (lambda v: v[..., :h, :]), (lambda v: v[..., h:, :])
    bf, f32 = jnp.bfloat16, jnp.float32
    up, down = _shift(n, axis, +1), _shift(n, axis, -1)
    from_behind = lax.ppermute(jnp.concatenate([lo(c[1]), hi(c[2])], axis=-2).astype(bf), "tensor", up)
    from_ahead = lax.ppermute(jnp.concatenate([lo(c[2]), hi(c[3])], axis=-2).astype(bf), "tensor", down)
    relay_up = (hi(c[1]).astype(f32) + hi(from_behind).astype(f32)).astype(bf)
    relay_down = (lo(c[3]).astype(f32) + lo(from_ahead).astype(f32)).astype(bf)
    second_behind = lax.ppermute(relay_up, "tensor", up)
    second_ahead = lax.ppermute(relay_down, "tensor", down)
    own = c[0].astype(f32)
    sum_lo = lo(own) + lo(from_behind).astype(f32) + second_ahead.astype(f32)
    sum_hi = hi(own) + hi(from_ahead).astype(f32) + second_behind.astype(f32)
    return jnp.concatenate([sum_lo, sum_hi], axis=-2)


def _ffn(rows, gate_weight, up_weight, down_weight):
    dims = (((1,), (1,)), ((), ()))
    gate = lax.dot_general(rows, gate_weight, dims, preferred_element_type=jnp.float32)
    up = lax.dot_general(rows, up_weight, dims, preferred_element_type=jnp.float32)
    act = (jax.nn.silu(gate) * up).astype(jnp.bfloat16)
    act = lax.optimization_barrier(act)
    return jnp.dot(act, down_weight, preferred_element_type=jnp.float32).astype(jnp.bfloat16)


def shards(hidden_rows, norm_gain, gate_weight, up_weight, down_weight, span_lengths):
    capacity, width = hidden_rows.shape
    n = span_lengths.shape[0]
    own_rank = lax.axis_index("tensor")
    widened = hidden_rows.astype(jnp.float32)
    scale = lax.rsqrt(jnp.mean(widened * widened, axis=-1, keepdims=True) + 1e-06)
    normed = (widened * scale * norm_gain).astype(jnp.bfloat16)

    half = capacity // 2

    def ffn(parts):
        rows = jnp.concatenate([p.reshape(-1, width) for p in parts], axis=0)
        out = _ffn(rows, gate_weight, up_weight, down_weight)
        pieces, at = [], 0
        for p in parts:
            count = p.size // width
            pieces.append(out[at:at + count].reshape(p.shape))
            at += count
        return pieces

    a_x = jnp.stack(_gather_ring(normed[:half], n, "x"))
    b_y = jnp.stack(_gather_ring(normed[half:], n, "y"))
    a0, a1, a2, a3 = _gather_ring(a_x, n, "y")
    b0, b1, b2, b3 = _gather_ring(b_y, n, "x")
    o_a0, o_b0 = ffn([a0, b0])
    o_a1, o_a3, o_b1, o_b3 = ffn([a1, a3, b1, b3])
    o_a2, o_b2 = ffn([a2, b2])
    out_a = [o_a0, o_a1, o_a2, o_a3]
    out_b = [o_b0, o_b1, o_b2, o_b3]

    sum_a = _reduce_relay(_reduce_relay(out_a, n, "y"), n, "x")
    sum_b = _reduce_relay(_reduce_relay(out_b, n, "x"), n, "y")
    result = jnp.concatenate([sum_a, sum_b], axis=0).astype(jnp.bfloat16)
    live_mask = jnp.arange(capacity, dtype=jnp.int32) < span_lengths[own_rank]
    return jnp.where(live_mask[:, None], result, jnp.zeros_like(result))


def solution(mesh):
    return jax.shard_map(
        shards,
        mesh=mesh,
        in_specs=(
            P(("dp", "tensor"), None),
            P(),
            P("tensor", None),
            P("tensor", None),
            P("tensor", None),
            P("dp"),
        ),
        out_specs=P(("dp", "tensor"), None),
        check_vma=False,
    )
```

```python
import jax
import jax.numpy as jnp
from jax import lax
from jax.sharding import PartitionSpec as P

NX = 4


def _shift(n, axis, step):
    ny = n // NX
    pairs = []
    for t in range(n):
        y, x = divmod(t, NX)
        if axis == "x":
            d = y * NX + (x + step) % NX
        else:
            d = ((y + step) % ny) * NX + x
        pairs.append((t, d))
    return pairs


def _halves(v):
    h = v.shape[0] // 2
    return (lambda u: u[:h]), (lambda u: u[h:])


def _gather_ring(s, n, axis):
    ahead = lax.ppermute(s, "tensor", _shift(n, axis, -1))
    behind = lax.ppermute(s, "tensor", _shift(n, axis, +1))
    lo, hi = _halves(s)
    far_lo = lax.ppermute(lo(behind), "tensor", _shift(n, axis, +1))
    far_hi = lax.ppermute(hi(ahead), "tensor", _shift(n, axis, -1))
    far = jnp.concatenate([far_lo, far_hi], axis=0)
    return [s, ahead, far, behind]


def _reduce_relay(c, n, axis):
    lo, hi = _halves(c[0])
    bf, f32 = jnp.bfloat16, jnp.float32
    up, down = _shift(n, axis, +1), _shift(n, axis, -1)
    from_behind = lax.ppermute(jnp.concatenate([lo(c[1]), hi(c[2])], axis=0).astype(bf), "tensor", up)
    from_ahead = lax.ppermute(jnp.concatenate([lo(c[2]), hi(c[3])], axis=0).astype(bf), "tensor", down)
    relay_up = (hi(c[1]).astype(f32) + hi(from_behind).astype(f32)).astype(bf)
    relay_down = (lo(c[3]).astype(f32) + lo(from_ahead).astype(f32)).astype(bf)
    second_behind = lax.ppermute(relay_up, "tensor", up)
    second_ahead = lax.ppermute(relay_down, "tensor", down)
    own = c[0].astype(f32)
    sum_lo = lo(own) + lo(from_behind).astype(f32) + second_ahead.astype(f32)
    sum_hi = hi(own) + hi(from_ahead).astype(f32) + second_behind.astype(f32)
    return jnp.concatenate([sum_lo, sum_hi], axis=0)


def _ffn(rows, gate_weight, up_weight, down_weight):
    dims = (((1,), (1,)), ((), ()))
    gate = lax.dot_general(rows, gate_weight, dims, preferred_element_type=jnp.float32)
    up = lax.dot_general(rows, up_weight, dims, preferred_element_type=jnp.float32)
    act = (jax.nn.silu(gate) * up).astype(jnp.bfloat16)
    act = lax.optimization_barrier(act)
    return jnp.dot(act, down_weight, preferred_element_type=jnp.float32).astype(jnp.bfloat16)


def shards(hidden_rows, norm_gain, gate_weight, up_weight, down_weight, span_lengths):
    capacity, width = hidden_rows.shape
    n = span_lengths.shape[0]
    own_rank = lax.axis_index("tensor")
    widened = hidden_rows.astype(jnp.float32)
    scale = lax.rsqrt(jnp.mean(widened * widened, axis=-1, keepdims=True) + 1e-06)
    normed = (widened * scale * norm_gain).astype(jnp.bfloat16)

    half = capacity // 2
    quarter = half // 2

    def ffn(parts):
        rows = jnp.concatenate([p.reshape(-1, width) for p in parts], axis=0)
        out = _ffn(rows, gate_weight, up_weight, down_weight)
        pieces, at = [], 0
        for p in parts:
            count = p.size // width
            pieces.append(out[at:at + count].reshape(p.shape))
            at += count
        return pieces

    def gather(a_rows, b_rows):
        a_x = jnp.stack(_gather_ring(a_rows, n, "x"))
        b_y = jnp.stack(_gather_ring(b_rows, n, "y"))
        return _gather_ring(a_x, n, "y"), _gather_ring(b_y, n, "x")

    def finish(a_parts, b_parts):
        a0, a1, a2, a3 = a_parts
        b0, b1, b2, b3 = b_parts
        o_a0, o_b0 = ffn([a0, b0])
        o_a1, o_a3, o_b1, o_b3 = ffn([a1, a3, b1, b3])
        o_a2, o_b2 = ffn([a2, b2])
        sum_a = _reduce_relay(_reduce_relay([o_a0, o_a1, o_a2, o_a3], n, "y"), n, "x")
        sum_b = _reduce_relay(_reduce_relay([o_b0, o_b1, o_b2, o_b3], n, "x"), n, "y")
        return sum_a, sum_b

    first = gather(normed[:quarter], normed[half:half + quarter])
    rest, first = lax.optimization_barrier(((normed[quarter:half], normed[half + quarter:]), first))
    second = gather(*rest)
    sum_a1, sum_b1 = finish(*first)
    sum_a2, sum_b2 = finish(*second)
    sum_a = jnp.concatenate([sum_a1, sum_a2], axis=0)
    sum_b = jnp.concatenate([sum_b1, sum_b2], axis=0)
    result = jnp.concatenate([sum_a, sum_b], axis=0).astype(jnp.bfloat16)
    live_mask = jnp.arange(capacity, dtype=jnp.int32) < span_lengths[own_rank]
    return jnp.where(live_mask[:, None], result, jnp.zeros_like(result))


def solution(mesh):
    return jax.shard_map(
        shards,
        mesh=mesh,
        in_specs=(
            P(("dp", "tensor"), None),
            P(),
            P("tensor", None),
            P("tensor", None),
            P("tensor", None),
            P("dp"),
        ),
        out_specs=P(("dp", "tensor"), None),
        check_vma=False,
    )
```

```python
import jax
import jax.numpy as jnp
from jax import lax
from jax.sharding import PartitionSpec as P

NX = 4


def _shift(n, axis, step):
    ny = n // NX
    pairs = []
    for t in range(n):
        y, x = divmod(t, NX)
        if axis == "x":
            d = y * NX + (x + step) % NX
        else:
            d = ((y + step) % ny) * NX + x
        pairs.append((t, d))
    return pairs


def _gather_ring(s, n, axis):
    ahead = lax.ppermute(s, "tensor", _shift(n, axis, -1))
    behind = lax.ppermute(s, "tensor", _shift(n, axis, +1))
    h = s.shape[-2] // 2
    far_lo = lax.ppermute(behind[..., :h, :], "tensor", _shift(n, axis, +1))
    far_hi = lax.ppermute(ahead[..., h:, :], "tensor", _shift(n, axis, -1))
    far = jnp.concatenate([far_lo, far_hi], axis=-2)
    return [s, ahead, far, behind]


def _reduce_relay(c, n, axis):
    h = c[0].shape[-2] // 2
    lo, hi = (lambda v: v[..., :h, :]), (lambda v: v[..., h:, :])
    bf, f32 = jnp.bfloat16, jnp.float32
    up, down = _shift(n, axis, +1), _shift(n, axis, -1)
    from_behind = lax.ppermute(jnp.concatenate([lo(c[1]), hi(c[2])], axis=-2).astype(bf), "tensor", up)
    from_ahead = lax.ppermute(jnp.concatenate([lo(c[2]), hi(c[3])], axis=-2).astype(bf), "tensor", down)
    relay_up = (hi(c[1]).astype(f32) + hi(from_behind).astype(f32)).astype(bf)
    relay_down = (lo(c[3]).astype(f32) + lo(from_ahead).astype(f32)).astype(bf)
    second_behind = lax.ppermute(relay_up, "tensor", up)
    second_ahead = lax.ppermute(relay_down, "tensor", down)
    own = c[0].astype(f32)
    sum_lo = lo(own) + lo(from_behind).astype(f32) + second_ahead.astype(f32)
    sum_hi = hi(own) + hi(from_ahead).astype(f32) + second_behind.astype(f32)
    return jnp.concatenate([sum_lo, sum_hi], axis=-2)


def _ffn(rows, gate_weight, up_weight, down_weight):
    dims = (((1,), (1,)), ((), ()))
    gate = lax.dot_general(rows, gate_weight, dims, preferred_element_type=jnp.float32)
    up = lax.dot_general(rows, up_weight, dims, preferred_element_type=jnp.float32)
    act = (jax.nn.silu(gate) * up).astype(jnp.bfloat16)
    act = lax.optimization_barrier(act)
    return jnp.dot(act, down_weight, preferred_element_type=jnp.float32).astype(jnp.bfloat16)


def shards(hidden_rows, norm_gain, gate_weight, up_weight, down_weight, span_lengths):
    capacity, width = hidden_rows.shape
    n = span_lengths.shape[0]
    own_rank = lax.axis_index("tensor")
    widened = hidden_rows.astype(jnp.float32)
    scale = lax.rsqrt(jnp.mean(widened * widened, axis=-1, keepdims=True) + 1e-06)
    normed = (widened * scale * norm_gain).astype(jnp.bfloat16)

    half = capacity // 2

    def ffn(part):
        return _ffn(part.reshape(-1, width), gate_weight, up_weight, down_weight).reshape(part.shape)

    a_x = jnp.stack(_gather_ring(normed[:half], n, "x"))
    b_y = jnp.stack(_gather_ring(normed[half:], n, "y"))
    a0, a1, a2, a3 = _gather_ring(a_x, n, "y")
    b0, b1, b2, b3 = _gather_ring(b_y, n, "x")
    far = ffn(jnp.stack([a2, b2]))
    out_a = [ffn(a0), ffn(a1), far[0], ffn(a3)]
    out_b = [ffn(b0), ffn(b1), far[1], ffn(b3)]

    sum_a = _reduce_relay(_reduce_relay(out_a, n, "y"), n, "x")
    sum_b = _reduce_relay(_reduce_relay(out_b, n, "x"), n, "y")
    result = jnp.concatenate([sum_a, sum_b], axis=0).astype(jnp.bfloat16)
    live_mask = jnp.arange(capacity, dtype=jnp.int32) < span_lengths[own_rank]
    return jnp.where(live_mask[:, None], result, jnp.zeros_like(result))


def solution(mesh):
    return jax.shard_map(
        shards,
        mesh=mesh,
        in_specs=(
            P(("dp", "tensor"), None),
            P(),
            P("tensor", None),
            P("tensor", None),
            P("tensor", None),
            P("dp"),
        ),
        out_specs=P(("dp", "tensor"), None),
        check_vma=False,
    )
```

```python
import jax
import jax.numpy as jnp
from jax import lax
from jax.sharding import PartitionSpec as P

NX = 4


def _shift(n, axis, step):
    ny = n // NX
    pairs = []
    for t in range(n):
        y, x = divmod(t, NX)
        if axis == "x":
            d = y * NX + (x + step) % NX
        else:
            d = ((y + step) % ny) * NX + x
        pairs.append((t, d))
    return pairs


def _gather_ring(s, n, axis):
    ahead = lax.ppermute(s, "tensor", _shift(n, axis, -1))
    behind = lax.ppermute(s, "tensor", _shift(n, axis, +1))
    h = s.shape[-2] // 2
    far_lo = lax.ppermute(behind[..., :h, :], "tensor", _shift(n, axis, +1))
    far_hi = lax.ppermute(ahead[..., h:, :], "tensor", _shift(n, axis, -1))
    far = jnp.concatenate([far_lo, far_hi], axis=-2)
    return [s, ahead, far, behind]


def _reduce_relay(c, n, axis):
    h = c[0].shape[-2] // 2
    lo, hi = (lambda v: v[..., :h, :]), (lambda v: v[..., h:, :])
    bf, f32 = jnp.bfloat16, jnp.float32
    up, down = _shift(n, axis, +1), _shift(n, axis, -1)
    from_behind = lax.ppermute(jnp.concatenate([lo(c[1]), hi(c[2])], axis=-2).astype(bf), "tensor", up)
    from_ahead = lax.ppermute(jnp.concatenate([lo(c[2]), hi(c[3])], axis=-2).astype(bf), "tensor", down)
    relay_up = (hi(c[1]).astype(f32) + hi(from_behind).astype(f32)).astype(bf)
    relay_down = (lo(c[3]).astype(f32) + lo(from_ahead).astype(f32)).astype(bf)
    second_behind = lax.ppermute(relay_up, "tensor", up)
    second_ahead = lax.ppermute(relay_down, "tensor", down)
    own = c[0].astype(f32)
    sum_lo = lo(own) + lo(from_behind).astype(f32) + second_ahead.astype(f32)
    sum_hi = hi(own) + hi(from_ahead).astype(f32) + second_behind.astype(f32)
    return jnp.concatenate([sum_lo, sum_hi], axis=-2)


def _ffn(rows, gate_weight, up_weight, down_weight):
    dims = (((1,), (1,)), ((), ()))
    gate = lax.dot_general(rows, gate_weight, dims, preferred_element_type=jnp.float32)
    up = lax.dot_general(rows, up_weight, dims, preferred_element_type=jnp.float32)
    act = (jax.nn.silu(gate) * up).astype(jnp.bfloat16)
    act = lax.optimization_barrier(act)
    return jnp.dot(act, down_weight, preferred_element_type=jnp.float32).astype(jnp.bfloat16)


def shards(hidden_rows, norm_gain, gate_weight, up_weight, down_weight, span_lengths):
    capacity, width = hidden_rows.shape
    n = span_lengths.shape[0]
    own_rank = lax.axis_index("tensor")
    widened = hidden_rows.astype(jnp.float32)
    scale = lax.rsqrt(jnp.mean(widened * widened, axis=-1, keepdims=True) + 1e-06)
    normed = (widened * scale * norm_gain).astype(jnp.bfloat16)

    half = capacity // 2

    def ffn(part):
        return _ffn(part.reshape(-1, width), gate_weight, up_weight, down_weight).reshape(part.shape)

    a_x = jnp.stack(_gather_ring(normed[:half], n, "x"))
    b_y = jnp.stack(_gather_ring(normed[half:], n, "y"))
    a0, a1, a2, a3 = _gather_ring(a_x, n, "y")
    b0, b1, b2, b3 = _gather_ring(b_y, n, "x")
    near_a = ffn(jnp.stack([a1, a3]))
    near_b = ffn(jnp.stack([b1, b3]))
    far = ffn(jnp.stack([a2, b2]))
    out_a = [ffn(a0), near_a[0], far[0], near_a[1]]
    out_b = [ffn(b0), near_b[0], far[1], near_b[1]]

    sum_a = _reduce_relay(_reduce_relay(out_a, n, "y"), n, "x")
    sum_b = _reduce_relay(_reduce_relay(out_b, n, "x"), n, "y")
    result = jnp.concatenate([sum_a, sum_b], axis=0).astype(jnp.bfloat16)
    live_mask = jnp.arange(capacity, dtype=jnp.int32) < span_lengths[own_rank]
    return jnp.where(live_mask[:, None], result, jnp.zeros_like(result))


def solution(mesh):
    return jax.shard_map(
        shards,
        mesh=mesh,
        in_specs=(
            P(("dp", "tensor"), None),
            P(),
            P("tensor", None),
            P("tensor", None),
            P("tensor", None),
            P("dp"),
        ),
        out_specs=P(("dp", "tensor"), None),
        check_vma=False,
    )
```

```python
import jax
import jax.numpy as jnp
from jax import lax
from jax.sharding import PartitionSpec as P

NX = 4


def _shift(n, axis, step):
    ny = n // NX
    pairs = []
    for t in range(n):
        y, x = divmod(t, NX)
        if axis == "x":
            d = y * NX + (x + step) % NX
        else:
            d = ((y + step) % ny) * NX + x
        pairs.append((t, d))
    return pairs


def _gather_ring(s, n, axis):
    ahead = lax.ppermute(s, "tensor", _shift(n, axis, -1))
    behind = lax.ppermute(s, "tensor", _shift(n, axis, +1))
    h = s.shape[-2] // 2
    far_lo = lax.ppermute(behind[..., :h, :], "tensor", _shift(n, axis, +1))
    far_hi = lax.ppermute(ahead[..., h:, :], "tensor", _shift(n, axis, -1))
    far = jnp.concatenate([far_lo, far_hi], axis=-2)
    return [s, ahead, far, behind]


def _reduce_relay(c, n, axis):
    h = c[0].shape[-2] // 2
    lo, hi = (lambda v: v[..., :h, :]), (lambda v: v[..., h:, :])
    bf, f32 = jnp.bfloat16, jnp.float32
    up, down = _shift(n, axis, +1), _shift(n, axis, -1)
    from_behind = lax.ppermute(jnp.concatenate([lo(c[1]), hi(c[2])], axis=-2).astype(bf), "tensor", up)
    from_ahead = lax.ppermute(jnp.concatenate([lo(c[2]), hi(c[3])], axis=-2).astype(bf), "tensor", down)
    relay_up = (hi(c[1]).astype(f32) + hi(from_behind).astype(f32)).astype(bf)
    relay_down = (lo(c[3]).astype(f32) + lo(from_ahead).astype(f32)).astype(bf)
    second_behind = lax.ppermute(relay_up, "tensor", up)
    second_ahead = lax.ppermute(relay_down, "tensor", down)
    own = c[0].astype(f32)
    sum_lo = lo(own) + lo(from_behind).astype(f32) + second_ahead.astype(f32)
    sum_hi = hi(own) + hi(from_ahead).astype(f32) + second_behind.astype(f32)
    return jnp.concatenate([sum_lo, sum_hi], axis=-2)


def _reduce_direct(c, n, axis):
    bf, f32 = jnp.bfloat16, jnp.float32
    from_behind = lax.ppermute(c[1].astype(bf), "tensor", _shift(n, axis, +1))
    from_ahead = lax.ppermute(c[3].astype(bf), "tensor", _shift(n, axis, -1))
    from_far = lax.ppermute(c[2].astype(bf), "tensor", _shift(n, axis, +2))
    return c[0].astype(f32) + from_behind.astype(f32) + from_ahead.astype(f32) + from_far.astype(f32)


def _ffn(rows, gate_weight, up_weight, down_weight):
    dims = (((1,), (1,)), ((), ()))
    gate = lax.dot_general(rows, gate_weight, dims, preferred_element_type=jnp.float32)
    up = lax.dot_general(rows, up_weight, dims, preferred_element_type=jnp.float32)
    act = (jax.nn.silu(gate) * up).astype(jnp.bfloat16)
    act = lax.optimization_barrier(act)
    return jnp.dot(act, down_weight, preferred_element_type=jnp.float32).astype(jnp.bfloat16)


def shards(hidden_rows, norm_gain, gate_weight, up_weight, down_weight, span_lengths):
    capacity, width = hidden_rows.shape
    n = span_lengths.shape[0]
    own_rank = lax.axis_index("tensor")
    widened = hidden_rows.astype(jnp.float32)
    scale = lax.rsqrt(jnp.mean(widened * widened, axis=-1, keepdims=True) + 1e-06)
    normed = (widened * scale * norm_gain).astype(jnp.bfloat16)

    half = capacity // 2

    def ffn(part):
        return _ffn(part.reshape(-1, width), gate_weight, up_weight, down_weight).reshape(part.shape)

    a_x = jnp.stack(_gather_ring(normed[:half], n, "x"))
    b_y = jnp.stack(_gather_ring(normed[half:], n, "y"))
    a0, a1, a2, a3 = _gather_ring(a_x, n, "y")
    b0, b1, b2, b3 = _gather_ring(b_y, n, "x")
    near_a = ffn(jnp.stack([a1, a3]))
    near_b = ffn(jnp.stack([b1, b3]))
    far = ffn(jnp.stack([a2, b2]))
    out_a = [ffn(a0), near_a[0], far[0], near_a[1]]
    out_b = [ffn(b0), near_b[0], far[1], near_b[1]]

    sum_a = _reduce_direct(_reduce_relay(out_a, n, "y"), n, "x")
    sum_b = _reduce_direct(_reduce_relay(out_b, n, "x"), n, "y")
    result = jnp.concatenate([sum_a, sum_b], axis=0).astype(jnp.bfloat16)
    live_mask = jnp.arange(capacity, dtype=jnp.int32) < span_lengths[own_rank]
    return jnp.where(live_mask[:, None], result, jnp.zeros_like(result))


def solution(mesh):
    return jax.shard_map(
        shards,
        mesh=mesh,
        in_specs=(
            P(("dp", "tensor"), None),
            P(),
            P("tensor", None),
            P("tensor", None),
            P("tensor", None),
            P("dp"),
        ),
        out_specs=P(("dp", "tensor"), None),
        check_vma=False,
    )
```

```python
import jax
import jax.numpy as jnp
from jax import lax
from jax.sharding import PartitionSpec as P

NX = 4


def _shift(n, axis, step):
    ny = n // NX
    pairs = []
    for t in range(n):
        y, x = divmod(t, NX)
        if axis == "x":
            d = y * NX + (x + step) % NX
        else:
            d = ((y + step) % ny) * NX + x
        pairs.append((t, d))
    return pairs


def _gather_ring(s, n, axis):
    ahead = lax.ppermute(s, "tensor", _shift(n, axis, -1))
    behind = lax.ppermute(s, "tensor", _shift(n, axis, +1))
    h = s.shape[-2] // 2
    far_lo = lax.ppermute(behind[..., :h, :], "tensor", _shift(n, axis, +1))
    far_hi = lax.ppermute(ahead[..., h:, :], "tensor", _shift(n, axis, -1))
    far = jnp.concatenate([far_lo, far_hi], axis=-2)
    return [s, ahead, far, behind]


def _gather_direct(s, n, axis):
    ahead = lax.ppermute(s, "tensor", _shift(n, axis, -1))
    behind = lax.ppermute(s, "tensor", _shift(n, axis, +1))
    far = lax.ppermute(s, "tensor", _shift(n, axis, +2))
    return [s, ahead, far, behind]


def _reduce_relay(c, n, axis):
    h = c[0].shape[-2] // 2
    lo, hi = (lambda v: v[..., :h, :]), (lambda v: v[..., h:, :])
    bf, f32 = jnp.bfloat16, jnp.float32
    up, down = _shift(n, axis, +1), _shift(n, axis, -1)
    from_behind = lax.ppermute(jnp.concatenate([lo(c[1]), hi(c[2])], axis=-2).astype(bf), "tensor", up)
    from_ahead = lax.ppermute(jnp.concatenate([lo(c[2]), hi(c[3])], axis=-2).astype(bf), "tensor", down)
    relay_up = (hi(c[1]).astype(f32) + hi(from_behind).astype(f32)).astype(bf)
    relay_down = (lo(c[3]).astype(f32) + lo(from_ahead).astype(f32)).astype(bf)
    second_behind = lax.ppermute(relay_up, "tensor", up)
    second_ahead = lax.ppermute(relay_down, "tensor", down)
    own = c[0].astype(f32)
    sum_lo = lo(own) + lo(from_behind).astype(f32) + second_ahead.astype(f32)
    sum_hi = hi(own) + hi(from_ahead).astype(f32) + second_behind.astype(f32)
    return jnp.concatenate([sum_lo, sum_hi], axis=-2)


def _reduce_direct(c, n, axis):
    bf, f32 = jnp.bfloat16, jnp.float32
    from_behind = lax.ppermute(c[1].astype(bf), "tensor", _shift(n, axis, +1))
    from_ahead = lax.ppermute(c[3].astype(bf), "tensor", _shift(n, axis, -1))
    from_far = lax.ppermute(c[2].astype(bf), "tensor", _shift(n, axis, +2))
    return c[0].astype(f32) + from_behind.astype(f32) + from_ahead.astype(f32) + from_far.astype(f32)


def _ffn(rows, gate_weight, up_weight, down_weight):
    dims = (((1,), (1,)), ((), ()))
    gate = lax.dot_general(rows, gate_weight, dims, preferred_element_type=jnp.float32)
    up = lax.dot_general(rows, up_weight, dims, preferred_element_type=jnp.float32)
    act = (jax.nn.silu(gate) * up).astype(jnp.bfloat16)
    act = lax.optimization_barrier(act)
    return jnp.dot(act, down_weight, preferred_element_type=jnp.float32).astype(jnp.bfloat16)


def shards(hidden_rows, norm_gain, gate_weight, up_weight, down_weight, span_lengths):
    capacity, width = hidden_rows.shape
    n = span_lengths.shape[0]
    own_rank = lax.axis_index("tensor")
    widened = hidden_rows.astype(jnp.float32)
    scale = lax.rsqrt(jnp.mean(widened * widened, axis=-1, keepdims=True) + 1e-06)
    normed = (widened * scale * norm_gain).astype(jnp.bfloat16)

    half = capacity // 2

    def ffn(part):
        return _ffn(part.reshape(-1, width), gate_weight, up_weight, down_weight).reshape(part.shape)

    a_x = jnp.stack(_gather_direct(normed[:half], n, "x"))
    b_y = jnp.stack(_gather_direct(normed[half:], n, "y"))
    a0, a1, a2, a3 = _gather_ring(a_x, n, "y")
    b0, b1, b2, b3 = _gather_ring(b_y, n, "x")
    near_a = ffn(jnp.stack([a1, a3]))
    near_b = ffn(jnp.stack([b1, b3]))
    far = ffn(jnp.stack([a2, b2]))
    out_a = [ffn(a0), near_a[0], far[0], near_a[1]]
    out_b = [ffn(b0), near_b[0], far[1], near_b[1]]

    sum_a = _reduce_direct(_reduce_relay(out_a, n, "y"), n, "x")
    sum_b = _reduce_direct(_reduce_relay(out_b, n, "x"), n, "y")
    result = jnp.concatenate([sum_a, sum_b], axis=0).astype(jnp.bfloat16)
    live_mask = jnp.arange(capacity, dtype=jnp.int32) < span_lengths[own_rank]
    return jnp.where(live_mask[:, None], result, jnp.zeros_like(result))


def solution(mesh):
    return jax.shard_map(
        shards,
        mesh=mesh,
        in_specs=(
            P(("dp", "tensor"), None),
            P(),
            P("tensor", None),
            P("tensor", None),
            P("tensor", None),
            P("dp"),
        ),
        out_specs=P(("dp", "tensor"), None),
        check_vma=False,
    )
```

```python
import jax
import jax.numpy as jnp
from jax import lax
from jax.sharding import PartitionSpec as P

NX = 4


def _shift(n, axis, step):
    ny = n // NX
    pairs = []
    for t in range(n):
        y, x = divmod(t, NX)
        if axis == "x":
            d = y * NX + (x + step) % NX
        else:
            d = ((y + step) % ny) * NX + x
        pairs.append((t, d))
    return pairs


def _gather_ring(s, n, axis):
    ahead = lax.ppermute(s, "tensor", _shift(n, axis, -1))
    behind = lax.ppermute(s, "tensor", _shift(n, axis, +1))
    h = s.shape[-2] // 2
    far_lo = lax.ppermute(behind[..., :h, :], "tensor", _shift(n, axis, +1))
    far_hi = lax.ppermute(ahead[..., h:, :], "tensor", _shift(n, axis, -1))
    far = jnp.concatenate([far_lo, far_hi], axis=-2)
    return [s, ahead, far, behind]


def _gather_direct(s, n, axis):
    ahead = lax.ppermute(s, "tensor", _shift(n, axis, -1))
    behind = lax.ppermute(s, "tensor", _shift(n, axis, +1))
    far = lax.ppermute(s, "tensor", _shift(n, axis, +2))
    return [s, ahead, far, behind]


def _reduce_relay(c, n, axis):
    h = c[0].shape[-2] // 2
    lo, hi = (lambda v: v[..., :h, :]), (lambda v: v[..., h:, :])
    bf, f32 = jnp.bfloat16, jnp.float32
    up, down = _shift(n, axis, +1), _shift(n, axis, -1)
    from_behind = lax.ppermute(jnp.concatenate([lo(c[1]), hi(c[2])], axis=-2).astype(bf), "tensor", up)
    from_ahead = lax.ppermute(jnp.concatenate([lo(c[2]), hi(c[3])], axis=-2).astype(bf), "tensor", down)
    relay_up = (hi(c[1]).astype(f32) + hi(from_behind).astype(f32)).astype(bf)
    relay_down = (lo(c[3]).astype(f32) + lo(from_ahead).astype(f32)).astype(bf)
    second_behind = lax.ppermute(relay_up, "tensor", up)
    second_ahead = lax.ppermute(relay_down, "tensor", down)
    own = c[0].astype(f32)
    sum_lo = lo(own) + lo(from_behind).astype(f32) + second_ahead.astype(f32)
    sum_hi = hi(own) + hi(from_ahead).astype(f32) + second_behind.astype(f32)
    return jnp.concatenate([sum_lo, sum_hi], axis=-2)


def _reduce_direct(c, n, axis):
    bf, f32 = jnp.bfloat16, jnp.float32
    from_behind = lax.ppermute(c[1].astype(bf), "tensor", _shift(n, axis, +1))
    from_ahead = lax.ppermute(c[3].astype(bf), "tensor", _shift(n, axis, -1))
    from_far = lax.ppermute(c[2].astype(bf), "tensor", _shift(n, axis, +2))
    return c[0].astype(f32) + from_behind.astype(f32) + from_ahead.astype(f32) + from_far.astype(f32)


def _ffn(rows, gate_weight, up_weight, down_weight):
    dims = (((1,), (1,)), ((), ()))
    gate = lax.dot_general(rows, gate_weight, dims, preferred_element_type=jnp.float32)
    up = lax.dot_general(rows, up_weight, dims, preferred_element_type=jnp.float32)
    act = (jax.nn.silu(gate) * up).astype(jnp.bfloat16)
    act = lax.optimization_barrier(act)
    return jnp.dot(act, down_weight, preferred_element_type=jnp.float32).astype(jnp.bfloat16)


def shards(hidden_rows, norm_gain, gate_weight, up_weight, down_weight, span_lengths):
    capacity, width = hidden_rows.shape
    n = span_lengths.shape[0]
    own_rank = lax.axis_index("tensor")
    widened = hidden_rows.astype(jnp.float32)
    scale = lax.rsqrt(jnp.mean(widened * widened, axis=-1, keepdims=True) + 1e-06)
    normed = (widened * scale * norm_gain).astype(jnp.bfloat16)

    half = capacity // 2

    def ffn(part):
        return _ffn(part.reshape(-1, width), gate_weight, up_weight, down_weight).reshape(part.shape)

    a_x = jnp.stack(_gather_direct(normed[:half], n, "x"))
    b_y = jnp.stack(_gather_direct(normed[half:], n, "y"))
    a0, a1, a2, a3 = _gather_ring(a_x, n, "y")
    b0, b1, b2, b3 = _gather_ring(b_y, n, "x")
    near_a = ffn(jnp.stack([a1, a3]))
    near_b = ffn(jnp.stack([b1, b3]))
    far = ffn(jnp.stack([a2, b2]))
    own = ffn(jnp.stack([a0, b0]))
    out_a = [own[0], near_a[0], far[0], near_a[1]]
    out_b = [own[1], near_b[0], far[1], near_b[1]]

    sum_a = _reduce_direct(_reduce_relay(out_a, n, "y"), n, "x")
    sum_b = _reduce_direct(_reduce_relay(out_b, n, "x"), n, "y")
    result = jnp.concatenate([sum_a, sum_b], axis=0).astype(jnp.bfloat16)
    live_mask = jnp.arange(capacity, dtype=jnp.int32) < span_lengths[own_rank]
    return jnp.where(live_mask[:, None], result, jnp.zeros_like(result))


def solution(mesh):
    return jax.shard_map(
        shards,
        mesh=mesh,
        in_specs=(
            P(("dp", "tensor"), None),
            P(),
            P("tensor", None),
            P("tensor", None),
            P("tensor", None),
            P("dp"),
        ),
        out_specs=P(("dp", "tensor"), None),
        check_vma=False,
    )
```

```python
import jax
import jax.numpy as jnp
from jax import lax
from jax.sharding import PartitionSpec as P

NX = 4


def _shift(n, axis, step):
    ny = n // NX
    pairs = []
    for t in range(n):
        y, x = divmod(t, NX)
        if axis == "x":
            d = y * NX + (x + step) % NX
        else:
            d = ((y + step) % ny) * NX + x
        pairs.append((t, d))
    return pairs


def _gather_ring(s, n, axis):
    ahead = lax.ppermute(s, "tensor", _shift(n, axis, -1))
    behind = lax.ppermute(s, "tensor", _shift(n, axis, +1))
    h = s.shape[-2] // 2
    far_lo = lax.ppermute(behind[..., :h, :], "tensor", _shift(n, axis, +1))
    far_hi = lax.ppermute(ahead[..., h:, :], "tensor", _shift(n, axis, -1))
    far = jnp.concatenate([far_lo, far_hi], axis=-2)
    return [s, ahead, far, behind]


def _gather_direct(s, n, axis):
    ahead = lax.ppermute(s, "tensor", _shift(n, axis, -1))
    behind = lax.ppermute(s, "tensor", _shift(n, axis, +1))
    far = lax.ppermute(s, "tensor", _shift(n, axis, +2))
    return [s, ahead, far, behind]


def _reduce_relay(c, n, axis):
    h = c[0].shape[-2] // 2
    lo, hi = (lambda v: v[..., :h, :]), (lambda v: v[..., h:, :])
    bf, f32 = jnp.bfloat16, jnp.float32
    up, down = _shift(n, axis, +1), _shift(n, axis, -1)
    from_behind = lax.ppermute(jnp.concatenate([lo(c[1]), hi(c[2])], axis=-2).astype(bf), "tensor", up)
    from_ahead = lax.ppermute(jnp.concatenate([lo(c[2]), hi(c[3])], axis=-2).astype(bf), "tensor", down)
    relay_up = (hi(c[1]).astype(f32) + hi(from_behind).astype(f32)).astype(bf)
    relay_down = (lo(c[3]).astype(f32) + lo(from_ahead).astype(f32)).astype(bf)
    second_behind = lax.ppermute(relay_up, "tensor", up)
    second_ahead = lax.ppermute(relay_down, "tensor", down)
    own = c[0].astype(f32)
    sum_lo = lo(own) + lo(from_behind).astype(f32) + second_ahead.astype(f32)
    sum_hi = hi(own) + hi(from_ahead).astype(f32) + second_behind.astype(f32)
    return jnp.concatenate([sum_lo, sum_hi], axis=-2)


def _reduce_direct(c, n, axis):
    bf, f32 = jnp.bfloat16, jnp.float32
    from_behind = lax.ppermute(c[1].astype(bf), "tensor", _shift(n, axis, +1))
    from_ahead = lax.ppermute(c[3].astype(bf), "tensor", _shift(n, axis, -1))
    from_far = lax.ppermute(c[2].astype(bf), "tensor", _shift(n, axis, +2))
    return c[0].astype(f32) + from_behind.astype(f32) + from_ahead.astype(f32) + from_far.astype(f32)


def _ffn(rows, gate_weight, up_weight, down_weight):
    dims = (((1,), (1,)), ((), ()))
    gate = lax.dot_general(rows, gate_weight, dims, preferred_element_type=jnp.float32)
    up = lax.dot_general(rows, up_weight, dims, preferred_element_type=jnp.float32)
    act = (jax.nn.silu(gate) * up).astype(jnp.bfloat16)
    act = lax.optimization_barrier(act)
    return jnp.dot(act, down_weight, preferred_element_type=jnp.float32).astype(jnp.bfloat16)


def shards(hidden_rows, norm_gain, gate_weight, up_weight, down_weight, span_lengths):
    capacity, width = hidden_rows.shape
    n = span_lengths.shape[0]
    own_rank = lax.axis_index("tensor")
    widened = hidden_rows.astype(jnp.float32)
    scale = lax.rsqrt(jnp.mean(widened * widened, axis=-1, keepdims=True) + 1e-06)
    normed = (widened * scale * norm_gain).astype(jnp.bfloat16)

    half = capacity // 2

    def ffn(part):
        return _ffn(part.reshape(-1, width), gate_weight, up_weight, down_weight).reshape(part.shape)

    a_x = jnp.stack(_gather_direct(normed[:half], n, "x"))
    b_y = jnp.stack(_gather_direct(normed[half:], n, "y"))
    a0, a1, a2, a3 = _gather_ring(a_x, n, "y")
    b0, b1, b2, b3 = _gather_ring(b_y, n, "x")
    near = ffn(jnp.stack([a1, a3, b1, b3]))
    far = ffn(jnp.stack([a2, b2]))
    own = ffn(jnp.stack([a0, b0]))
    out_a = [own[0], near[0], far[0], near[1]]
    out_b = [own[1], near[2], far[1], near[3]]

    sum_a = _reduce_direct(_reduce_relay(out_a, n, "y"), n, "x")
    sum_b = _reduce_direct(_reduce_relay(out_b, n, "x"), n, "y")
    result = jnp.concatenate([sum_a, sum_b], axis=0).astype(jnp.bfloat16)
    live_mask = jnp.arange(capacity, dtype=jnp.int32) < span_lengths[own_rank]
    return jnp.where(live_mask[:, None], result, jnp.zeros_like(result))


def solution(mesh):
    return jax.shard_map(
        shards,
        mesh=mesh,
        in_specs=(
            P(("dp", "tensor"), None),
            P(),
            P("tensor", None),
            P("tensor", None),
            P("tensor", None),
            P("dp"),
        ),
        out_specs=P(("dp", "tensor"), None),
        check_vma=False,
    )
```

```python
import jax
import jax.numpy as jnp
from jax import lax
from jax.sharding import PartitionSpec as P

NX = 4


def _shift(n, axis, step):
    ny = n // NX
    pairs = []
    for t in range(n):
        y, x = divmod(t, NX)
        if axis == "x":
            d = y * NX + (x + step) % NX
        else:
            d = ((y + step) % ny) * NX + x
        pairs.append((t, d))
    return pairs


def _gather_ring(s, n, axis):
    ahead = lax.ppermute(s, "tensor", _shift(n, axis, -1))
    behind = lax.ppermute(s, "tensor", _shift(n, axis, +1))
    h = s.shape[-2] // 2
    far_lo = lax.ppermute(behind[..., :h, :], "tensor", _shift(n, axis, +1))
    far_hi = lax.ppermute(ahead[..., h:, :], "tensor", _shift(n, axis, -1))
    far = jnp.concatenate([far_lo, far_hi], axis=-2)
    return [s, ahead, far, behind]


def _gather_direct(s, n, axis):
    ahead = lax.ppermute(s, "tensor", _shift(n, axis, -1))
    behind = lax.ppermute(s, "tensor", _shift(n, axis, +1))
    far = lax.ppermute(s, "tensor", _shift(n, axis, +2))
    return [s, ahead, far, behind]


def _reduce_relay(c, n, axis, split_far=False):
    h = c[0].shape[-2] // 2
    lo, hi = (lambda v: v[..., :h, :]), (lambda v: v[..., h:, :])
    bf, f32 = jnp.bfloat16, jnp.float32
    up, down = _shift(n, axis, +1), _shift(n, axis, -1)
    if split_far:
        far_behind = lax.ppermute(hi(c[2]).astype(bf), "tensor", up)
        far_ahead = lax.ppermute(lo(c[2]).astype(bf), "tensor", down)
        near_behind = lax.ppermute(lo(c[1]).astype(bf), "tensor", up)
        near_ahead = lax.ppermute(hi(c[3]).astype(bf), "tensor", down)
    else:
        from_behind = lax.ppermute(jnp.concatenate([lo(c[1]), hi(c[2])], axis=-2).astype(bf), "tensor", up)
        from_ahead = lax.ppermute(jnp.concatenate([lo(c[2]), hi(c[3])], axis=-2).astype(bf), "tensor", down)
        near_behind, far_behind = lo(from_behind), hi(from_behind)
        far_ahead, near_ahead = lo(from_ahead), hi(from_ahead)
    relay_up = (hi(c[1]).astype(f32) + far_behind.astype(f32)).astype(bf)
    relay_down = (lo(c[3]).astype(f32) + far_ahead.astype(f32)).astype(bf)
    second_behind = lax.ppermute(relay_up, "tensor", up)
    second_ahead = lax.ppermute(relay_down, "tensor", down)
    own = c[0].astype(f32)
    sum_lo = lo(own) + near_behind.astype(f32) + second_ahead.astype(f32)
    sum_hi = hi(own) + near_ahead.astype(f32) + second_behind.astype(f32)
    return jnp.concatenate([sum_lo, sum_hi], axis=-2)


def _reduce_direct(c, n, axis):
    bf, f32 = jnp.bfloat16, jnp.float32
    from_behind = lax.ppermute(c[1].astype(bf), "tensor", _shift(n, axis, +1))
    from_ahead = lax.ppermute(c[3].astype(bf), "tensor", _shift(n, axis, -1))
    from_far = lax.ppermute(c[2].astype(bf), "tensor", _shift(n, axis, +2))
    return c[0].astype(f32) + from_behind.astype(f32) + from_ahead.astype(f32) + from_far.astype(f32)


def _ffn(rows, gate_weight, up_weight, down_weight):
    dims = (((1,), (1,)), ((), ()))
    gate = lax.dot_general(rows, gate_weight, dims, preferred_element_type=jnp.float32)
    up = lax.dot_general(rows, up_weight, dims, preferred_element_type=jnp.float32)
    act = (jax.nn.silu(gate) * up).astype(jnp.bfloat16)
    act = lax.optimization_barrier(act)
    return jnp.dot(act, down_weight, preferred_element_type=jnp.float32).astype(jnp.bfloat16)


def shards(hidden_rows, norm_gain, gate_weight, up_weight, down_weight, span_lengths):
    capacity, width = hidden_rows.shape
    n = span_lengths.shape[0]
    own_rank = lax.axis_index("tensor")
    widened = hidden_rows.astype(jnp.float32)
    scale = lax.rsqrt(jnp.mean(widened * widened, axis=-1, keepdims=True) + 1e-06)
    normed = (widened * scale * norm_gain).astype(jnp.bfloat16)

    half = capacity // 2

    def ffn(part):
        return _ffn(part.reshape(-1, width), gate_weight, up_weight, down_weight).reshape(part.shape)

    a_x = jnp.stack(_gather_direct(normed[:half], n, "x"))
    b_y = jnp.stack(_gather_direct(normed[half:], n, "y"))
    a0, a1, a2, a3 = _gather_ring(a_x, n, "y")
    b0, b1, b2, b3 = _gather_ring(b_y, n, "x")
    near = ffn(jnp.stack([a1, a3, b1, b3]))
    far = ffn(jnp.stack([a2, b2]))
    own = ffn(jnp.stack([a0, b0]))
    out_a = [own[0], near[0], far[0], near[1]]
    out_b = [own[1], near[2], far[1], near[3]]

    sum_a = _reduce_direct(_reduce_relay(out_a, n, "y"), n, "x")
    sum_b = _reduce_direct(_reduce_relay(out_b, n, "x", split_far=True), n, "y")
    result = jnp.concatenate([sum_a, sum_b], axis=0).astype(jnp.bfloat16)
    live_mask = jnp.arange(capacity, dtype=jnp.int32) < span_lengths[own_rank]
    return jnp.where(live_mask[:, None], result, jnp.zeros_like(result))


def solution(mesh):
    return jax.shard_map(
        shards,
        mesh=mesh,
        in_specs=(
            P(("dp", "tensor"), None),
            P(),
            P("tensor", None),
            P("tensor", None),
            P("tensor", None),
            P("dp"),
        ),
        out_specs=P(("dp", "tensor"), None),
        check_vma=False,
    )
```
